512 devices in a mesh: fit: 32 (over z, core), orb: 16 (over x, y).
Axes of the slice: x: 4, y: 4, z: 16, core: 2. Of those that a mesh axis runs over, the one named last changes fastest.
Arguments:
- half_ints: bfloat16 [16, 256, 768, 256], P('orb', None, 'fit'), may hold values from -6 to 6
- osv_coef: bfloat16 [16, 256, 256, 64], P('orb', 'fit'), may hold values from -0.09375 to 0.09375
- fit_blocks: int32 [16, 256, 6], P('orb', 'fit'), may hold values from 0 to 468, as said below
- partner_list: int32 [32, 16, 24], P('fit'), may hold values from 0 to 127, as said below
Outputs:
- pair_ints: bfloat16 [16, 256, 24, 4096], P('orb', 'fit')
The draws below stay inside these ranges and needn't reach their ends.
Inputs may be any that keep to these rules, and one draw needn't show every extreme that they name: `fit_blocks`: the 6 block numbers of one orbital are distinct. `partner_list`: entry h * 8 + k names orbital k of the same column in group h. The 24 entries of one list are distinct. Of one list, at most 3 entries name orbitals of any one group, and in every list some group is named exactly 3 times.
All inputs are finite; a program needn't handle non-finite values.
Results may differ from the reference program's by a relative error of at most 0.0055.
Values may be sent and summed in bfloat16 or wider, within the bound.
No kernel may reach another device: no remote copies, remote signals or barrier semaphores. Data moves between devices by JAX's collectives and lax.ppermute only.
A program may use at most 64 MiB of HBM per device.

```python
import jax
import jax.numpy as jnp
from jax import lax

AOD = 256
BLK = 128
FBLK = 6
NOSV = 64
NFB = 469
ORB_DEV = 8
NPART = 24
FD = 768
ORBITAL_GROUPS = 16
GROUP_COLUMNS = 32
GRP = 256
CAP = 3


def draw_fit_blocks(key, part):
    key_pool, key_pick = jax.random.split(key)
    pool_size = 2 * FBLK
    scores = jax.random.randint(key_pool, (NFB,), 0, 1 << 20) * 1024 + jnp.arange(NFB, dtype=jnp.int32)
    pool_ids = jnp.argsort(scores)[:pool_size].astype(jnp.int32)
    pick_scores = jax.random.randint(key_pick, (ORBITAL_GROUPS, GRP, pool_size), 0, 1 << 20) * 64 + jnp.arange(pool_size, dtype=jnp.int32)
    chosen_order = jnp.argsort(pick_scores, axis=-1)[..., :FBLK]
    return pool_ids[chosen_order].astype(jnp.int32)


def draw_partner_list(key, part):
    popular_key, key_forced, key_base, key_perm = jax.random.split(key, 4)
    slot_count = ORBITAL_GROUPS * CAP
    slot_positions = jnp.arange(slot_count, dtype=jnp.int32)
    slot_holder = slot_positions // CAP
    popular_boost = jax.random.randint(popular_key, (GROUP_COLUMNS, ORBITAL_GROUPS), 0, 3)
    mandatory_flags = jax.random.randint(key_forced, (GROUP_COLUMNS, ORBITAL_GROUPS), 0, ORBITAL_GROUPS)
    baseline_sample = jax.random.randint(key_base, (GROUP_COLUMNS, ORBITAL_GROUPS, slot_count), 0, 4096)
    holder_boost = popular_boost[:, slot_holder][:, None, :]
    mandatory_boost = (slot_holder[None, None, :] == mandatory_flags[:, :, None]).astype(jnp.int32) * 8
    ranking_score = (baseline_sample + (holder_boost + mandatory_boost) * 4096) * 1024 + slot_positions[None, None, :]
    top_vals, chosen = lax.top_k(ranking_score, NPART)
    owner_group = chosen // CAP
    slot_within = chosen % CAP
    perm_scores = jax.random.randint(key_perm, (GROUP_COLUMNS, ORBITAL_GROUPS, ORBITAL_GROUPS, ORB_DEV), 0, 1 << 20) * 64 + jnp.arange(ORB_DEV, dtype=jnp.int32)
    local_perm = jnp.argsort(perm_scores, axis=-1).astype(jnp.int32).reshape(GROUP_COLUMNS, ORBITAL_GROUPS, ORBITAL_GROUPS * ORB_DEV)
    local_pick = jnp.take_along_axis(local_perm, owner_group * ORB_DEV + slot_within, axis=2)
    return (owner_group * ORB_DEV + local_pick).astype(jnp.int32)


def levels(stream_key, extent, cuts, low, top_value):
    level = 1.0
    for axis_at, shards_of in cuts:
        steps = jax.random.uniform(jax.random.fold_in(jax.random.fold_in(stream_key, 6), axis_at), (shards_of,), jnp.float32, low / len(cuts), top_value / len(cuts))
        level = level * jnp.repeat(jnp.exp(steps), extent[axis_at] // shards_of).reshape((-1,) + (1,) * (len(extent) - 1 - axis_at))
    return level


def noise(rng, shape, spread, bound, cuts=(), kind=jnp.bfloat16):
    gain = levels(rng, shape, cuts, -0.22, 0.18) if cuts else 1.0
    values = jax.random.normal(rng, shape, jnp.float32) * spread * gain
    return jnp.minimum(jnp.maximum(values, -bound), bound).astype(kind)


def setup_inputs(seed: int = 0) -> dict:
    streams_of = jax.random.split(jax.random.key(seed), 5)
    return {
        "half_ints": noise(streams_of[0], (ORBITAL_GROUPS, GRP, FD, AOD), 1.0, 6.0, ((0, 16), (2, 32))),
        "osv_coef": noise(streams_of[1], (ORBITAL_GROUPS, GRP, AOD, NOSV), (AOD * 16) ** -0.5, 0.09375, ((0, 16), (1, 32))),
        "fit_blocks": draw_fit_blocks(jax.random.fold_in(streams_of[4], 71), 0),
        "partner_list": draw_partner_list(jax.random.fold_in(streams_of[4], 71), 0),
    }


def pair_block(own_rows, own_ids, partner_rows, partner_ids):
    matching = (own_ids[None, :, None] == partner_ids[:, None, :]).astype(jnp.float32)
    pieces = partner_rows.astype(jnp.float32).reshape(NPART, NOSV, FBLK, BLK)
    aligned = jnp.einsum('nbc,nxcp->nxbp', matching, pieces).astype(jnp.bfloat16)
    local_rows = own_rows.astype(jnp.float32).reshape(NOSV, FBLK, BLK)
    pair_vals = jnp.einsum('abp,nxbp->nax', local_rows, aligned.astype(jnp.float32))
    return pair_vals.reshape(NPART, NOSV * NOSV).astype(jnp.bfloat16)


def reference(half_ints, osv_coef, fit_blocks, partner_list):
    def project(operand):
        group_rows, group_coef = operand
        return jnp.einsum('rfa,rao->rof', group_rows.astype(jnp.float32), group_coef.astype(jnp.float32)).astype(jnp.bfloat16)

    projected = lax.map(project, (half_ints, osv_coef))
    flat_rows = projected.reshape(ORBITAL_GROUPS * GRP, NOSV, FD)
    flat_blocks = fit_blocks.reshape(ORBITAL_GROUPS * GRP, FBLK)

    def one_orbital(orbital):
        group = orbital // GRP
        row_index = orbital % GRP
        column = row_index // ORB_DEV
        wanted = partner_list[column, group]
        partner_ids = ((wanted // ORB_DEV) * GRP + column * ORB_DEV + wanted % ORB_DEV).astype(jnp.int32)
        return pair_block(flat_rows[orbital], flat_blocks[orbital], flat_rows[partner_ids], flat_blocks[partner_ids])

    result = lax.map(one_orbital, jnp.arange(ORBITAL_GROUPS * GRP, dtype=jnp.int32))
    return result.reshape(ORBITAL_GROUPS, GRP, NPART, NOSV * NOSV)
```

```python
import jax
import jax.numpy as jnp
import numpy as np
from jax import lax
from jax.sharding import Mesh, PartitionSpec as P

BLK = 128
FBLK = 6
CAP = 3
ORB_DEV = 8


def per_device(half_ints, osv_coef, fit_blocks, partner_list):
    nz = lax.axis_size("z")
    ncore = lax.axis_size("core")
    rows = half_ints[0]
    n_orb, fchunk, aod = rows.shape
    rows = rows.reshape(nz, ncore, n_orb // (nz * ncore), fchunk, aod)
    mine = lax.all_to_all(rows, "core", split_axis=1, concat_axis=3, tiled=True)
    mine = mine.reshape(nz, n_orb // (nz * ncore), ncore * fchunk, aod)
    coef = lax.all_gather(osv_coef[0], "z", axis=0, tiled=False)
    part = jnp.einsum(
        "zkfm,zkma->zkaf", mine, coef, preferred_element_type=jnp.float32
    ).astype(jnp.bfloat16)
    projected = lax.all_to_all(part, "z", split_axis=0, concat_axis=3, tiled=True)[0]
    n_loc, nosv, fd = projected.shape

    own_blocks = fit_blocks[0]
    lists = partner_list[0]
    ngroups, npart = lists.shape
    owner = lists // ORB_DEV
    sub = lists % ORB_DEV
    earlier = jnp.tril(jnp.ones((npart, npart), jnp.int32), -1)
    same = (owner[:, :, None] == owner[:, None, :]).astype(jnp.int32)
    rank = jnp.sum(same * earlier[None], axis=2)
    me = lax.axis_index("orb")
    sel = (
        (owner == me)[:, :, None, None]
        & (rank[:, :, None, None] == jnp.arange(CAP)[None, None, :, None])
        & (sub[:, :, None, None] == jnp.arange(n_loc)[None, None, None, :])
    )
    sel = jnp.sum(sel.astype(jnp.float32), axis=1).astype(jnp.bfloat16)
    code = jnp.concatenate(
        [own_blocks // 8, own_blocks % 8, jnp.zeros((n_loc, 128 - 2 * FBLK), jnp.int32)], axis=1
    ).astype(jnp.bfloat16)
    payload = jnp.concatenate([projected.reshape(n_loc, nosv * fd), code], axis=1)
    send = jnp.einsum("dsk,kv->dsv", sel, payload, preferred_element_type=jnp.float32).astype(
        jnp.bfloat16
    )
    recv = lax.all_to_all(send, "orb", split_axis=0, concat_axis=0, tiled=True)
    recv = recv.reshape(ngroups * CAP, -1)
    my_owner = lax.dynamic_index_in_dim(owner, me, 0, keepdims=False)
    my_rank = lax.dynamic_index_in_dim(rank, me, 0, keepdims=False)
    slot = my_owner * CAP + my_rank
    pick = (slot[:, None] == jnp.arange(ngroups * CAP)[None, :]).astype(jnp.bfloat16)
    partner = jnp.einsum("ns,sv->nv", pick, recv, preferred_element_type=jnp.float32)
    pcode = partner[:, nosv * fd : nosv * fd + 2 * FBLK]
    pblocks = (pcode[:, :FBLK] * 8 + pcode[:, FBLK:]).astype(jnp.int32)
    prow = partner[:, : nosv * fd].astype(jnp.bfloat16).reshape(npart, nosv, FBLK, BLK)

    match = (own_blocks[:, None, :, None] == pblocks[None, :, None, :]).astype(jnp.bfloat16)
    aligned = jnp.einsum(
        "rnbe,nxep->rnxbp", match, prow, preferred_element_type=jnp.float32
    ).astype(jnp.bfloat16)
    pair = jnp.einsum(
        "rabp,rnxbp->rnax",
        projected.reshape(n_loc, nosv, FBLK, BLK),
        aligned,
        preferred_element_type=jnp.float32,
    ).astype(jnp.bfloat16)
    return pair.reshape(1, n_loc, npart, nosv * nosv)


def solution(mesh):
    nfit = mesh.shape["fit"]
    norb = mesh.shape["orb"]
    devs = np.asarray(mesh.devices).reshape(nfit // 2, 2, norb)
    mesh3 = Mesh(devs, ("z", "core", "orb"))
    fit = ("z", "core")
    return jax.shard_map(
        per_device,
        mesh=mesh3,
        in_specs=(
            P("orb", None, fit, None),
            P("orb", fit, None, None),
            P("orb", fit, None),
            P(fit, None, None),
        ),
        out_specs=P("orb", fit, None, None),
        check_vma=False,
    )
```

```python
import jax
import jax.numpy as jnp
import numpy as np
from jax import lax
from jax.sharding import Mesh, PartitionSpec as P

BLK = 128
FBLK = 6
CAP = 3
ORB_DEV = 8


NSTAGE = 2


def per_device(half_ints, osv_coef, fit_blocks, partner_list):
    nz = lax.axis_size("z")
    ncore = lax.axis_size("core")
    rows = half_ints[0]
    n_orb, fchunk, aod = rows.shape
    n_loc = n_orb // (nz * ncore)
    rows = rows.reshape(nz, ncore, n_loc, fchunk, aod)
    mine = lax.all_to_all(rows, "core", split_axis=1, concat_axis=3, tiled=True)
    mine = mine.reshape(nz, n_loc, ncore * fchunk, aod)
    coef_all = osv_coef[0]
    nosv = coef_all.shape[-1]
    hs = nosv // NSTAGE
    fd = ncore * fchunk * nz

    own_blocks = fit_blocks[0]
    lists = partner_list[0]
    ngroups, npart = lists.shape
    owner = lists // ORB_DEV
    sub = lists % ORB_DEV
    earlier = jnp.tril(jnp.ones((npart, npart), jnp.int32), -1)
    same = (owner[:, :, None] == owner[:, None, :]).astype(jnp.int32)
    rank = jnp.sum(same * earlier[None], axis=2)
    me = lax.axis_index("orb")
    sel = (
        (owner == me)[:, :, None, None]
        & (rank[:, :, None, None] == jnp.arange(CAP)[None, None, :, None])
        & (sub[:, :, None, None] == jnp.arange(n_loc)[None, None, None, :])
    )
    sel = jnp.sum(sel.astype(jnp.float32), axis=1).astype(jnp.bfloat16)
    my_owner = lax.dynamic_index_in_dim(owner, me, 0, keepdims=False)
    my_rank = lax.dynamic_index_in_dim(rank, me, 0, keepdims=False)
    slot = my_owner * CAP + my_rank
    pick = (slot[:, None] == jnp.arange(ngroups * CAP)[None, :]).astype(jnp.bfloat16)
    code = jnp.concatenate(
        [own_blocks // 8, own_blocks % 8, jnp.zeros((n_loc, 128 - 2 * FBLK), jnp.int32)], axis=1
    ).astype(jnp.bfloat16)

    own_parts = []
    partner_parts = []
    pblocks = None
    for h in range(NSTAGE):
        coef = lax.all_gather(coef_all[:, :, h * hs : (h + 1) * hs], "z", axis=0, tiled=False)
        part = jnp.einsum(
            "zkfm,zkma->zkaf", mine, coef, preferred_element_type=jnp.float32
        ).astype(jnp.bfloat16)
        proj = lax.all_to_all(part, "z", split_axis=0, concat_axis=3, tiled=True)[0]
        own_parts.append(proj)
        payload = proj.reshape(n_loc, hs * fd)
        if h == 0:
            payload = jnp.concatenate([payload, code], axis=1)
        send = jnp.einsum(
            "dsk,kv->dsv", sel, payload, preferred_element_type=jnp.float32
        ).astype(jnp.bfloat16)
        recv = lax.all_to_all(send, "orb", split_axis=0, concat_axis=0, tiled=True)
        recv = recv.reshape(ngroups * CAP, -1)
        partner = jnp.einsum("ns,sv->nv", pick, recv, preferred_element_type=jnp.float32)
        if h == 0:
            pcode = partner[:, hs * fd : hs * fd + 2 * FBLK]
            pblocks = (pcode[:, :FBLK] * 8 + pcode[:, FBLK:]).astype(jnp.int32)
        partner_parts.append(
            partner[:, : hs * fd].astype(jnp.bfloat16).reshape(npart, hs, FBLK, BLK)
        )

    projected = jnp.concatenate(own_parts, axis=1)
    match = (own_blocks[:, None, :, None] == pblocks[None, :, None, :]).astype(jnp.bfloat16)
    outs = []
    for h in range(NSTAGE):
        aligned = jnp.einsum(
            "rnbe,nxep->rnxbp", match, partner_parts[h], preferred_element_type=jnp.float32
        ).astype(jnp.bfloat16)
        outs.append(
            jnp.einsum(
                "rabp,rnxbp->rnax",
                projected.reshape(n_loc, nosv, FBLK, BLK),
                aligned,
                preferred_element_type=jnp.float32,
            ).astype(jnp.bfloat16)
        )
    pair = jnp.concatenate(outs, axis=3)
    return pair.reshape(1, n_loc, npart, nosv * nosv)


def solution(mesh):
    nfit = mesh.shape["fit"]
    norb = mesh.shape["orb"]
    devs = np.asarray(mesh.devices).reshape(nfit // 2, 2, norb)
    mesh3 = Mesh(devs, ("z", "core", "orb"))
    fit = ("z", "core")
    return jax.shard_map(
        per_device,
        mesh=mesh3,
        in_specs=(
            P("orb", None, fit, None),
            P("orb", fit, None, None),
            P("orb", fit, None),
            P(fit, None, None),
        ),
        out_specs=P("orb", fit, None, None),
        check_vma=False,
    )
```

```python
import jax
import jax.numpy as jnp
import numpy as np
from jax import lax
from jax.sharding import Mesh, PartitionSpec as P

BLK = 128
FBLK = 6
CAP = 3
ORB_DEV = 8
KA = 4


def body(half_ints, osv_coef, fit_blocks, partner_list):
    nz = lax.axis_size("z")
    ncore = lax.axis_size("core")
    rows = half_ints[0]
    n_orb, fchunk, aod = rows.shape
    ncol = nz * ncore
    n_loc = n_orb // ncol
    rows = rows.reshape(ncol, n_loc, fchunk, aod)
    coef_own = osv_coef[0]
    rows_a = lax.all_to_all(rows[:, :KA], ("z", "core"), split_axis=0, concat_axis=2, tiled=True)
    proj_a = jnp.einsum(
        "kfm,kma->kaf", rows_a[0], coef_own[:KA], preferred_element_type=jnp.float32
    ).astype(jnp.bfloat16)
    rows_b = rows[:, KA:].reshape(nz, ncore, n_loc - KA, fchunk, aod)
    mine = lax.all_to_all(rows_b, "core", split_axis=1, concat_axis=3, tiled=True)
    mine = mine.reshape(nz, n_loc - KA, ncore * fchunk, aod)
    coef = lax.all_gather(coef_own[KA:], "z", axis=0, tiled=False)
    part = jnp.einsum(
        "zkfm,zkma->zkaf", mine, coef, preferred_element_type=jnp.float32
    ).astype(jnp.bfloat16)
    proj_b = lax.all_to_all(part, "z", split_axis=0, concat_axis=3, tiled=True)[0]
    projected = jnp.concatenate([proj_a, proj_b], axis=0)
    n_loc, nosv, fd = projected.shape

    own_blocks = fit_blocks[0]
    lists = partner_list[0]
    ngroups, npart = lists.shape
    owner = lists // ORB_DEV
    sub = lists % ORB_DEV
    earlier = jnp.tril(jnp.ones((npart, npart), jnp.int32), -1)
    same = (owner[:, :, None] == owner[:, None, :]).astype(jnp.int32)
    rank = jnp.sum(same * earlier[None], axis=2)
    me = lax.axis_index("orb")
    sel = (
        (owner == me)[:, :, None, None]
        & (rank[:, :, None, None] == jnp.arange(CAP)[None, None, :, None])
        & (sub[:, :, None, None] == jnp.arange(n_loc)[None, None, None, :])
    )
    sel = jnp.sum(sel.astype(jnp.float32), axis=1).astype(jnp.bfloat16)
    code = jnp.concatenate(
        [own_blocks // 8, own_blocks % 8, jnp.zeros((n_loc, 128 - 2 * FBLK), jnp.int32)], axis=1
    ).astype(jnp.bfloat16)
    payload = jnp.concatenate([projected.reshape(n_loc, nosv * fd), code], axis=1)
    send = jnp.einsum("dsk,kv->dsv", sel, payload, preferred_element_type=jnp.float32).astype(
        jnp.bfloat16
    )
    recv = lax.all_to_all(send, "orb", split_axis=0, concat_axis=0, tiled=True)
    recv = recv.reshape(ngroups * CAP, -1)
    my_owner = lax.dynamic_index_in_dim(owner, me, 0, keepdims=False)
    my_rank = lax.dynamic_index_in_dim(rank, me, 0, keepdims=False)
    slot = my_owner * CAP + my_rank
    pick = (slot[:, None] == jnp.arange(ngroups * CAP)[None, :]).astype(jnp.bfloat16)
    partner = jnp.einsum("ns,sv->nv", pick, recv, preferred_element_type=jnp.float32)
    pcode = partner[:, nosv * fd : nosv * fd + 2 * FBLK]
    pblocks = (pcode[:, :FBLK] * 8 + pcode[:, FBLK:]).astype(jnp.int32)
    prow = partner[:, : nosv * fd].astype(jnp.bfloat16).reshape(npart, nosv, FBLK, BLK)

    match = (own_blocks[:, None, :, None] == pblocks[None, :, None, :]).astype(jnp.bfloat16)
    aligned = jnp.einsum(
        "rnbe,nxep->rnxbp", match, prow, preferred_element_type=jnp.float32
    ).astype(jnp.bfloat16)
    pair = jnp.einsum(
        "rabp,rnxbp->rnax",
        projected.reshape(n_loc, nosv, FBLK, BLK),
        aligned,
        preferred_element_type=jnp.float32,
    ).astype(jnp.bfloat16)
    return pair.reshape(1, n_loc, npart, nosv * nosv)


def solution(mesh):
    nfit = mesh.shape["fit"]
    norb = mesh.shape["orb"]
    devs = np.asarray(mesh.devices).reshape(nfit // 2, 2, norb)
    mesh3 = Mesh(devs, ("z", "core", "orb"))
    fit = ("z", "core")
    return jax.shard_map(
        body,
        mesh=mesh3,
        in_specs=(
            P("orb", None, fit, None),
            P("orb", fit, None, None),
            P("orb", fit, None),
            P(fit, None, None),
        ),
        out_specs=P("orb", fit, None, None),
        check_vma=False,
    )
```

```python
import functools
import jax
import jax.numpy as jnp
import numpy as np
from jax import lax
from jax.experimental import pallas as pl
from jax.experimental.pallas import tpu as pltpu
from jax.sharding import Mesh, PartitionSpec as P

BLK = 128
FBLK = 6
CAP = 3
ORB_DEV = 8


def per_device(half_ints, osv_coef, fit_blocks, partner_list):
    nz = lax.axis_size("z")
    ncore = lax.axis_size("core")
    rows = half_ints[0]
    n_orb, fchunk, aod = rows.shape
    rows = rows.reshape(nz, ncore, n_orb // (nz * ncore), fchunk, aod)
    mine = lax.all_to_all(rows, "core", split_axis=1, concat_axis=3, tiled=True)
    mine = mine.reshape(nz, n_orb // (nz * ncore), ncore * fchunk, aod)
    coef = lax.all_gather(osv_coef[0], "z", axis=0, tiled=False)
    part = jnp.einsum(
        "zkfm,zkma->zkaf", mine, coef, preferred_element_type=jnp.float32
    ).astype(jnp.bfloat16)
    projected = lax.all_to_all(part, "z", split_axis=0, concat_axis=3, tiled=True)[0]
    n_loc, nosv, fd = projected.shape

    own_blocks = fit_blocks[0]
    lists = partner_list[0]
    ngroups, npart = lists.shape
    owner = lists // ORB_DEV
    sub = lists % ORB_DEV
    earlier = jnp.tril(jnp.ones((npart, npart), jnp.int32), -1)
    same = (owner[:, :, None] == owner[:, None, :]).astype(jnp.int32)
    rank = jnp.sum(same * earlier[None], axis=2)
    me = lax.axis_index("orb")
    sel = (
        (owner == me)[:, :, None, None]
        & (rank[:, :, None, None] == jnp.arange(CAP)[None, None, :, None])
        & (sub[:, :, None, None] == jnp.arange(n_loc)[None, None, None, :])
    )
    sel = jnp.sum(sel.astype(jnp.float32), axis=1).astype(jnp.bfloat16)
    nblk = fd // BLK
    code_rows = 8
    code = jnp.concatenate(
        [own_blocks // 8, own_blocks % 8, jnp.zeros((n_loc, BLK - 2 * FBLK), jnp.int32)], axis=1
    ).astype(jnp.bfloat16)
    code = jnp.concatenate(
        [code[:, None, :], jnp.zeros((n_loc, code_rows - 1, BLK), jnp.bfloat16)], axis=1
    )
    blocks_major = projected.reshape(n_loc, nosv, nblk, BLK).transpose(0, 2, 1, 3)
    payload = jnp.concatenate([blocks_major.reshape(n_loc, nblk * nosv, BLK), code], axis=1)
    send = jnp.einsum("dsk,kyp->dsyp", sel, payload, preferred_element_type=jnp.float32).astype(
        jnp.bfloat16
    )
    recv = lax.all_to_all(send, "orb", split_axis=0, concat_axis=0, tiled=True)
    recv = recv.reshape(ngroups * CAP, nblk * nosv + code_rows, BLK)
    my_owner = lax.dynamic_index_in_dim(owner, me, 0, keepdims=False)
    my_rank = lax.dynamic_index_in_dim(rank, me, 0, keepdims=False)
    slot = (my_owner * CAP + my_rank).astype(jnp.int32)
    pick = (slot[:, None] == jnp.arange(ngroups * CAP)[None, :]).astype(jnp.float32)
    codes = recv[:, nblk * nosv, : 2 * FBLK].astype(jnp.float32)
    pcode = jnp.einsum("ns,sc->nc", pick, codes)
    pblocks = (pcode[:, :FBLK] * 8 + pcode[:, FBLK:]).astype(jnp.int32)
    match = own_blocks[:, None, :, None] == pblocks[None, :, None, :]
    eidx = jnp.sum(jnp.where(match, jnp.arange(1, FBLK + 1)[None, None, None, :], 0), axis=3) - 1
    res = pair_call(slot, eidx.astype(jnp.int32).reshape(-1), projected, recv)
    pair = res.reshape(n_loc, nosv, npart, nosv).transpose(0, 2, 1, 3)
    return pair.reshape(1, n_loc, npart, nosv * nosv)


def pair_kernel(slot_ref, eidx_ref, own_ref, recv_ref, out_ref, a_ref, *, npart, nosv):
    r = pl.program_id(0)

    def fill(n, carry):
        s = slot_ref[n]
        for b in range(FBLK):
            e = eidx_ref[(r * npart + n) * FBLK + b]
            ee = jnp.maximum(e, 0)
            blk = recv_ref[s, pl.ds(pl.multiple_of(ee * nosv, nosv), nosv), :]
            blk = jnp.where(e >= 0, blk, jnp.zeros_like(blk))
            a_ref[pl.ds(pl.multiple_of(n * nosv, nosv), nosv), pl.ds(b * BLK, BLK)] = blk
        return carry

    lax.fori_loop(0, npart, fill, 0)
    res = lax.dot_general(
        own_ref[0], a_ref[...], (((1,), (1,)), ((), ())), preferred_element_type=jnp.float32
    )
    out_ref[0] = res.astype(out_ref.dtype)


def pair_call(slot, eidx, own, recv, interpret=False):
    n_loc, nosv, fd = own.shape
    npart = slot.shape[0]
    nslot, rows, _ = recv.shape
    kern = functools.partial(pair_kernel, npart=npart, nosv=nosv)
    return pl.pallas_call(
        kern,
        out_shape=jax.ShapeDtypeStruct((n_loc, nosv, npart * nosv), jnp.bfloat16),
        grid_spec=pltpu.PrefetchScalarGridSpec(
            num_scalar_prefetch=2,
            grid=(n_loc,),
            in_specs=[
                pl.BlockSpec((1, nosv, fd), lambda r, s, e: (r, 0, 0)),
                pl.BlockSpec((nslot, rows, BLK), lambda r, s, e: (0, 0, 0)),
            ],
            out_specs=pl.BlockSpec((1, nosv, npart * nosv), lambda r, s, e: (r, 0, 0)),
            scratch_shapes=[pltpu.VMEM((npart * nosv, fd), jnp.bfloat16)],
        ),
        interpret=interpret,
    )(slot, eidx, own, recv)


def solution(mesh):
    nfit = mesh.shape["fit"]
    norb = mesh.shape["orb"]
    devs = np.asarray(mesh.devices).reshape(nfit // 2, 2, norb)
    mesh3 = Mesh(devs, ("z", "core", "orb"))
    fit = ("z", "core")
    return jax.shard_map(
        per_device,
        mesh=mesh3,
        in_specs=(
            P("orb", None, fit, None),
            P("orb", fit, None, None),
            P("orb", fit, None),
            P(fit, None, None),
        ),
        out_specs=P("orb", fit, None, None),
        check_vma=False,
    )
```

```python
import functools
import jax
import jax.numpy as jnp
import numpy as np
from jax import lax
from jax.experimental import pallas as pl
from jax.experimental.pallas import tpu as pltpu
from jax.sharding import Mesh, PartitionSpec as P

BLK = 128
FBLK = 6
CAP = 3
ORB_DEV = 8


def per_device(half_ints, osv_coef, fit_blocks, partner_list):
    nz = lax.axis_size("z")
    ncore = lax.axis_size("core")
    rows = half_ints[0]
    n_orb, fchunk, aod = rows.shape
    rows = rows.reshape(nz, ncore, n_orb // (nz * ncore), fchunk, aod)
    mine = lax.all_to_all(rows, "core", split_axis=1, concat_axis=3, tiled=True)
    mine = mine.reshape(nz, n_orb // (nz * ncore), ncore * fchunk, aod)
    coef0 = osv_coef[0]
    zi = lax.axis_index("z")
    right = [(i, (i + 1) % nz) for i in range(nz)]
    left = [(i, (i - 1) % nz) for i in range(nz)]
    chunks = [None] * nz
    chunks[0] = coef0
    go_r = coef0
    go_l = coef0
    for t in range(1, nz // 2 + 1):
        go_r = lax.ppermute(go_r, "z", right)
        chunks[(nz - t) % nz] = go_r
        if t < nz - t:
            go_l = lax.ppermute(go_l, "z", left)
            chunks[t] = go_l
    parts = []
    for d in range(nz):
        rows_d = lax.dynamic_index_in_dim(mine, (zi + d) % nz, 0, keepdims=False)
        parts.append(
            jnp.einsum(
                "kfm,kma->kaf", rows_d, chunks[d], preferred_element_type=jnp.float32
            ).astype(jnp.bfloat16)
        )
    part_rel = jnp.stack(parts)
    doubled = jnp.concatenate([part_rel, part_rel], axis=0)
    part = lax.dynamic_slice_in_dim(doubled, (nz - zi) % nz, nz, 0)
    projected = lax.all_to_all(part, "z", split_axis=0, concat_axis=3, tiled=True)[0]
    n_loc, nosv, fd = projected.shape

    own_blocks = fit_blocks[0]
    lists = partner_list[0]
    ngroups, npart = lists.shape
    owner = lists // ORB_DEV
    sub = lists % ORB_DEV
    earlier = jnp.tril(jnp.ones((npart, npart), jnp.int32), -1)
    same = (owner[:, :, None] == owner[:, None, :]).astype(jnp.int32)
    rank = jnp.sum(same * earlier[None], axis=2)
    me = lax.axis_index("orb")
    sel = (
        (owner == me)[:, :, None, None]
        & (rank[:, :, None, None] == jnp.arange(CAP)[None, None, :, None])
        & (sub[:, :, None, None] == jnp.arange(n_loc)[None, None, None, :])
    )
    sel = jnp.sum(sel.astype(jnp.float32), axis=1).astype(jnp.bfloat16)
    nblk = fd // BLK
    code_rows = 8
    code = jnp.concatenate(
        [own_blocks // 8, own_blocks % 8, jnp.zeros((n_loc, BLK - 2 * FBLK), jnp.int32)], axis=1
    ).astype(jnp.bfloat16)
    code = jnp.concatenate(
        [code[:, None, :], jnp.zeros((n_loc, code_rows - 1, BLK), jnp.bfloat16)], axis=1
    )
    blocks_major = projected.reshape(n_loc, nosv, nblk, BLK).transpose(0, 2, 1, 3)
    payload = jnp.concatenate([blocks_major.reshape(n_loc, nblk * nosv, BLK), code], axis=1)
    send = jnp.einsum("dsk,kyp->dsyp", sel, payload, preferred_element_type=jnp.float32).astype(
        jnp.bfloat16
    )
    recv = lax.all_to_all(send, "orb", split_axis=0, concat_axis=0, tiled=True)
    recv = recv.reshape(ngroups * CAP, nblk * nosv + code_rows, BLK)
    my_owner = lax.dynamic_index_in_dim(owner, me, 0, keepdims=False)
    my_rank = lax.dynamic_index_in_dim(rank, me, 0, keepdims=False)
    slot = (my_owner * CAP + my_rank).astype(jnp.int32)
    pick = (slot[:, None] == jnp.arange(ngroups * CAP)[None, :]).astype(jnp.float32)
    codes = recv[:, nblk * nosv, : 2 * FBLK].astype(jnp.float32)
    pcode = jnp.einsum("ns,sc->nc", pick, codes)
    pblocks = (pcode[:, :FBLK] * 8 + pcode[:, FBLK:]).astype(jnp.int32)
    match = own_blocks[:, None, :, None] == pblocks[None, :, None, :]
    eidx = jnp.sum(jnp.where(match, jnp.arange(1, FBLK + 1)[None, None, None, :], 0), axis=3) - 1
    res = pair_call(slot, eidx.astype(jnp.int32).reshape(-1), projected, recv)
    pair = res.reshape(n_loc, nosv, npart, nosv).transpose(0, 2, 1, 3)
    return pair.reshape(1, n_loc, npart, nosv * nosv)


def pair_kernel(slot_ref, eidx_ref, own_ref, recv_ref, out_ref, a_ref, *, npart, nosv):
    r = pl.program_id(0)

    def fill(n, carry):
        s = slot_ref[n]
        for b in range(FBLK):
            e = eidx_ref[(r * npart + n) * FBLK + b]
            ee = jnp.maximum(e, 0)
            blk = recv_ref[s, pl.ds(pl.multiple_of(ee * nosv, nosv), nosv), :]
            blk = jnp.where(e >= 0, blk, jnp.zeros_like(blk))
            a_ref[pl.ds(pl.multiple_of(n * nosv, nosv), nosv), pl.ds(b * BLK, BLK)] = blk
        return carry

    lax.fori_loop(0, npart, fill, 0)
    res = lax.dot_general(
        own_ref[0], a_ref[...], (((1,), (1,)), ((), ())), preferred_element_type=jnp.float32
    )
    out_ref[0] = res.astype(out_ref.dtype)


def pair_call(slot, eidx, own, recv, interpret=False):
    n_loc, nosv, fd = own.shape
    npart = slot.shape[0]
    nslot, rows, _ = recv.shape
    kern = functools.partial(pair_kernel, npart=npart, nosv=nosv)
    return pl.pallas_call(
        kern,
        out_shape=jax.ShapeDtypeStruct((n_loc, nosv, npart * nosv), jnp.bfloat16),
        grid_spec=pltpu.PrefetchScalarGridSpec(
            num_scalar_prefetch=2,
            grid=(n_loc,),
            in_specs=[
                pl.BlockSpec((1, nosv, fd), lambda r, s, e: (r, 0, 0)),
                pl.BlockSpec((nslot, rows, BLK), lambda r, s, e: (0, 0, 0)),
            ],
            out_specs=pl.BlockSpec((1, nosv, npart * nosv), lambda r, s, e: (r, 0, 0)),
            scratch_shapes=[pltpu.VMEM((npart * nosv, fd), jnp.bfloat16)],
        ),
        interpret=interpret,
    )(slot, eidx, own, recv)


def solution(mesh):
    nfit = mesh.shape["fit"]
    norb = mesh.shape["orb"]
    devs = np.asarray(mesh.devices).reshape(nfit // 2, 2, norb)
    mesh3 = Mesh(devs, ("z", "core", "orb"))
    fit = ("z", "core")
    return jax.shard_map(
        per_device,
        mesh=mesh3,
        in_specs=(
            P("orb", None, fit, None),
            P("orb", fit, None, None),
            P("orb", fit, None),
            P(fit, None, None),
        ),
        out_specs=P("orb", fit, None, None),
        check_vma=False,
    )
```

```python
import functools
import jax
import jax.numpy as jnp
import numpy as np
from jax import lax
from jax.experimental import pallas as pl
from jax.experimental.pallas import tpu as pltpu
from jax.sharding import Mesh, PartitionSpec as P

BLK = 128
FBLK = 6
CAP = 3
ORB_DEV = 8


def per_device(half_ints, osv_coef, fit_blocks, partner_list):
    nz = lax.axis_size("z")
    ncore = lax.axis_size("core")
    rows = half_ints[0]
    n_orb, fchunk, aod = rows.shape
    rows = rows.reshape(nz, ncore, n_orb // (nz * ncore), fchunk, aod)
    mine = lax.all_to_all(rows, "core", split_axis=1, concat_axis=3, tiled=True)
    mine = mine.reshape(nz, n_orb // (nz * ncore), ncore * fchunk, aod)
    coef = lax.all_gather(osv_coef[0], "z", axis=0, tiled=False)
    part = jnp.einsum(
        "zkfm,zkma->zkaf", mine, coef, preferred_element_type=jnp.float32
    ).astype(jnp.bfloat16)
    projected = lax.all_to_all(part, "z", split_axis=0, concat_axis=3, tiled=True)[0]
    n_loc, nosv, fd = projected.shape

    own_blocks = fit_blocks[0]
    lists = partner_list[0]
    ngroups, npart = lists.shape
    owner = lists // ORB_DEV
    sub = lists % ORB_DEV
    earlier = jnp.tril(jnp.ones((npart, npart), jnp.int32), -1)
    same = (owner[:, :, None] == owner[:, None, :]).astype(jnp.int32)
    rank = jnp.sum(same * earlier[None], axis=2)
    me = lax.axis_index("orb")
    sel = (
        (owner == me)[:, :, None, None]
        & (rank[:, :, None, None] == jnp.arange(CAP)[None, None, :, None])
        & (sub[:, :, None, None] == jnp.arange(n_loc)[None, None, None, :])
    )
    sel = jnp.sum(sel.astype(jnp.float32), axis=1).astype(jnp.bfloat16)
    nblk = fd // BLK
    code_rows = 8
    code = jnp.concatenate(
        [own_blocks // 8, own_blocks % 8, jnp.zeros((n_loc, BLK - 2 * FBLK), jnp.int32)], axis=1
    ).astype(jnp.bfloat16)
    code = jnp.concatenate(
        [code[:, None, :], jnp.zeros((n_loc, code_rows - 1, BLK), jnp.bfloat16)], axis=1
    )
    blocks_major = projected.reshape(n_loc, nosv, nblk, BLK).transpose(0, 2, 1, 3)
    payload = jnp.concatenate([blocks_major.reshape(n_loc, nblk * nosv, BLK), code], axis=1)
    send = jnp.einsum("dsk,kyp->dsyp", sel, payload, preferred_element_type=jnp.float32).astype(
        jnp.bfloat16
    )
    recv = lax.all_to_all(send, "orb", split_axis=0, concat_axis=0, tiled=True)
    recv = recv.reshape(ngroups * CAP, nblk * nosv + code_rows, BLK)
    my_owner = lax.dynamic_index_in_dim(owner, me, 0, keepdims=False)
    my_rank = lax.dynamic_index_in_dim(rank, me, 0, keepdims=False)
    slot = (my_owner * CAP + my_rank).astype(jnp.int32)
    pick = (slot[:, None] == jnp.arange(ngroups * CAP)[None, :]).astype(jnp.float32)
    codes = recv[:, nblk * nosv, : 2 * FBLK].astype(jnp.float32)
    pcode = jnp.einsum("ns,sc->nc", pick, codes)
    pblocks = (pcode[:, :FBLK] * 8 + pcode[:, FBLK:]).astype(jnp.int32)
    match = pblocks[:, None, None, :] == own_blocks[None, :, :, None]
    bidx = jnp.sum(jnp.where(match, jnp.arange(1, FBLK + 1)[None, None, :, None], 0), axis=2) - 1
    pair = pair_call(slot, bidx.astype(jnp.int32).reshape(-1), blocks_major, recv)
    return pair.reshape(1, n_loc, npart, nosv * nosv)


def pair_kernel(slot_ref, bidx_ref, own_ref, recv_ref, out_ref, al_ref):
    n = pl.program_id(0)
    n_loc, nblk, nosv, _ = own_ref.shape
    s = slot_ref[n]
    for r in range(n_loc):
        for e in range(nblk):
            b = bidx_ref[(n * n_loc + r) * nblk + e]
            blk = own_ref[r, jnp.maximum(b, 0)]
            blk = jnp.where(b >= 0, blk, jnp.zeros_like(blk))
            al_ref[r * nosv : (r + 1) * nosv, e * BLK : (e + 1) * BLK] = blk
    part = jnp.concatenate(
        [recv_ref[s, e * nosv : (e + 1) * nosv, :] for e in range(nblk)], axis=1
    )
    res = lax.dot_general(
        al_ref[...], part, (((1,), (1,)), ((), ())), preferred_element_type=jnp.float32
    )
    out_ref[:, 0] = res.reshape(n_loc, nosv, nosv).astype(out_ref.dtype)


def pair_call(slot, bidx, own_bm, recv, interpret=False):
    n_loc, nblk, nosv, _ = own_bm.shape
    npart = slot.shape[0]
    nslot, rows, _ = recv.shape
    return pl.pallas_call(
        pair_kernel,
        out_shape=jax.ShapeDtypeStruct((n_loc, npart, nosv, nosv), jnp.bfloat16),
        grid_spec=pltpu.PrefetchScalarGridSpec(
            num_scalar_prefetch=2,
            grid=(npart,),
            in_specs=[
                pl.BlockSpec((n_loc, nblk, nosv, BLK), lambda n, s, b: (0, 0, 0, 0)),
                pl.BlockSpec((nslot, rows, BLK), lambda n, s, b: (0, 0, 0)),
            ],
            out_specs=pl.BlockSpec((n_loc, 1, nosv, nosv), lambda n, s, b: (0, n, 0, 0)),
            scratch_shapes=[pltpu.VMEM((n_loc * nosv, nblk * BLK), jnp.bfloat16)],
        ),
        interpret=interpret,
    )(slot, bidx, own_bm, recv)


def solution(mesh):
    nfit = mesh.shape["fit"]
    norb = mesh.shape["orb"]
    devs = np.asarray(mesh.devices).reshape(nfit // 2, 2, norb)
    mesh3 = Mesh(devs, ("z", "core", "orb"))
    fit = ("z", "core")
    return jax.shard_map(
        per_device,
        mesh=mesh3,
        in_specs=(
            P("orb", None, fit, None),
            P("orb", fit, None, None),
            P("orb", fit, None),
            P(fit, None, None),
        ),
        out_specs=P("orb", fit, None, None),
        check_vma=False,
    )
```

```python
import functools
import jax
import jax.numpy as jnp
import numpy as np
from jax import lax
from jax.experimental import pallas as pl
from jax.experimental.pallas import tpu as pltpu
from jax.sharding import Mesh, PartitionSpec as P

BLK = 128
FBLK = 6
CAP = 3
ORB_DEV = 8


def per_device(half_ints, osv_coef, fit_blocks, partner_list):
    nz = lax.axis_size("z")
    ncore = lax.axis_size("core")
    rows = half_ints[0]
    n_orb, fchunk, aod = rows.shape
    rows = rows.reshape(nz, ncore, n_orb // (nz * ncore), fchunk, aod)
    mine = lax.all_to_all(rows, "core", split_axis=1, concat_axis=3, tiled=True)
    mine = mine.reshape(nz, n_orb // (nz * ncore), ncore * fchunk, aod)
    coef = lax.all_gather(osv_coef[0], "z", axis=0, tiled=False)
    part = jnp.einsum(
        "zkfm,zkma->zkaf", mine, coef, preferred_element_type=jnp.float32
    ).astype(jnp.bfloat16)
    projected = lax.all_to_all(part, "z", split_axis=0, concat_axis=3, tiled=True)[0]
    n_loc, nosv, fd = projected.shape

    own_blocks = fit_blocks[0]
    lists = partner_list[0]
    ngroups, npart = lists.shape
    owner = lists // ORB_DEV
    sub = lists % ORB_DEV
    earlier = jnp.tril(jnp.ones((npart, npart), jnp.int32), -1)
    same = (owner[:, :, None] == owner[:, None, :]).astype(jnp.int32)
    rank = jnp.sum(same * earlier[None], axis=2)
    me = lax.axis_index("orb")
    sel = (
        (owner == me)[:, :, None, None]
        & (rank[:, :, None, None] == jnp.arange(CAP)[None, None, :, None])
        & (sub[:, :, None, None] == jnp.arange(n_loc)[None, None, None, :])
    )
    sel = jnp.sum(sel.astype(jnp.float32), axis=1).astype(jnp.bfloat16)
    nblk = fd // BLK
    code_rows = 8
    code = jnp.concatenate(
        [own_blocks // 8, own_blocks % 8, jnp.zeros((n_loc, BLK - 2 * FBLK), jnp.int32)], axis=1
    ).astype(jnp.bfloat16)
    code = jnp.concatenate(
        [code[:, None, :], jnp.zeros((n_loc, code_rows - 1, BLK), jnp.bfloat16)], axis=1
    )
    blocks_major = projected.reshape(n_loc, nosv, nblk, BLK).transpose(0, 2, 1, 3)
    payload = jnp.concatenate([blocks_major.reshape(n_loc, nblk * nosv, BLK), code], axis=1)
    send = jnp.einsum("dsk,kyp->dsyp", sel, payload, preferred_element_type=jnp.float32).astype(
        jnp.bfloat16
    )
    recv = lax.all_to_all(send, "orb", split_axis=0, concat_axis=0, tiled=True)
    recv = recv.reshape(ngroups * CAP, nblk * nosv + code_rows, BLK)
    my_owner = lax.dynamic_index_in_dim(owner, me, 0, keepdims=False)
    my_rank = lax.dynamic_index_in_dim(rank, me, 0, keepdims=False)
    slot = (my_owner * CAP + my_rank).astype(jnp.int32)
    pick = (slot[:, None] == jnp.arange(ngroups * CAP)[None, :]).astype(jnp.float32)
    codes = recv[:, nblk * nosv, : 2 * FBLK].astype(jnp.float32)
    pcode = jnp.einsum("ns,sc->nc", pick, codes)
    pblocks = (pcode[:, :FBLK] * 8 + pcode[:, FBLK:]).astype(jnp.int32)
    match = pblocks[:, None, None, :] == own_blocks[None, :, :, None]
    bidx = jnp.sum(jnp.where(match, jnp.arange(1, FBLK + 1)[None, None, :, None], 0), axis=2) - 1
    pair = pair_call(slot, bidx.astype(jnp.int32).reshape(-1), blocks_major, recv)
    return pair.reshape(1, n_loc, npart, nosv * nosv)


def make_pair_call(npb):
    def pair_kernel(slot_ref, bidx_ref, own_ref, recv_ref, out_ref, al_ref):
        g = pl.program_id(0)
        n_loc, nblk, nosv, _ = own_ref.shape
        for j in range(npb):
            n = g * npb + j
            s = slot_ref[n]
            for r in range(n_loc):
                for e in range(nblk):
                    b = bidx_ref[(n * n_loc + r) * nblk + e]
                    blk = own_ref[r, jnp.maximum(b, 0)]
                    blk = jnp.where(b >= 0, blk, jnp.zeros_like(blk))
                    al_ref[j, r * nosv : (r + 1) * nosv, e * BLK : (e + 1) * BLK] = blk
            part = jnp.concatenate(
                [recv_ref[s, e * nosv : (e + 1) * nosv, :] for e in range(nblk)], axis=1
            )
            res = lax.dot_general(
                al_ref[j], part, (((1,), (1,)), ((), ())), preferred_element_type=jnp.float32
            )
            out_ref[:, j] = res.reshape(n_loc, nosv, nosv).astype(out_ref.dtype)

    def pair_call(slot, bidx, own_bm, recv):
        n_loc, nblk, nosv, _ = own_bm.shape
        npart = slot.shape[0]
        nslot, rows, _ = recv.shape
        return pl.pallas_call(
            pair_kernel,
            out_shape=jax.ShapeDtypeStruct((n_loc, npart, nosv, nosv), jnp.bfloat16),
            grid_spec=pltpu.PrefetchScalarGridSpec(
                num_scalar_prefetch=2,
                grid=(npart // npb,),
                in_specs=[
                    pl.BlockSpec((n_loc, nblk, nosv, BLK), lambda g, s, b: (0, 0, 0, 0)),
                    pl.BlockSpec((nslot, rows, BLK), lambda g, s, b: (0, 0, 0)),
                ],
                out_specs=pl.BlockSpec((n_loc, npb, nosv, nosv), lambda g, s, b: (0, g, 0, 0)),
                scratch_shapes=[pltpu.VMEM((npb, n_loc * nosv, nblk * BLK), jnp.bfloat16)],
            ),
        )(slot, bidx, own_bm, recv)

    return pair_call


pair_call = make_pair_call(4)


def solution(mesh):
    nfit = mesh.shape["fit"]
    norb = mesh.shape["orb"]
    devs = np.asarray(mesh.devices).reshape(nfit // 2, 2, norb)
    mesh3 = Mesh(devs, ("z", "core", "orb"))
    fit = ("z", "core")
    return jax.shard_map(
        per_device,
        mesh=mesh3,
        in_specs=(
            P("orb", None, fit, None),
            P("orb", fit, None, None),
            P("orb", fit, None),
            P(fit, None, None),
        ),
        out_specs=P("orb", fit, None, None),
        check_vma=False,
    )
```

```python
import functools
import jax
import jax.numpy as jnp
import numpy as np
from jax import lax
from jax.experimental import pallas as pl
from jax.experimental.pallas import tpu as pltpu
from jax.sharding import Mesh, PartitionSpec as P

BLK = 128
FBLK = 6
CAP = 3
ORB_DEV = 8


def per_device(half_ints, osv_coef, fit_blocks, partner_list):
    nz = lax.axis_size("z")
    ncore = lax.axis_size("core")
    rows = half_ints[0]
    n_orb, fchunk, aod = rows.shape
    rows = rows.reshape(nz, ncore, n_orb // (nz * ncore), fchunk, aod)
    mine = lax.all_to_all(rows, "core", split_axis=1, concat_axis=3, tiled=True)
    mine = mine.reshape(nz, n_orb // (nz * ncore), ncore * fchunk, aod)
    coef = lax.all_gather(osv_coef[0], "z", axis=0, tiled=False)
    part = jnp.einsum(
        "zkfm,zkma->zkaf", mine, coef, preferred_element_type=jnp.float32
    ).astype(jnp.bfloat16)
    projected = lax.all_to_all(part, "z", split_axis=0, concat_axis=3, tiled=True)[0]
    n_loc, nosv, fd = projected.shape

    own_blocks = fit_blocks[0]
    lists = partner_list[0]
    ngroups, npart = lists.shape
    owner = lists // ORB_DEV
    sub = lists % ORB_DEV
    earlier = jnp.tril(jnp.ones((npart, npart), jnp.int32), -1)
    same = (owner[:, :, None] == owner[:, None, :]).astype(jnp.int32)
    rank = jnp.sum(same * earlier[None], axis=2)
    me = lax.axis_index("orb")
    sel = (
        (owner == me)[:, :, None, None]
        & (rank[:, :, None, None] == jnp.arange(CAP)[None, None, :, None])
        & (sub[:, :, None, None] == jnp.arange(n_loc)[None, None, None, :])
    )
    sel = jnp.sum(sel.astype(jnp.float32), axis=1).astype(jnp.bfloat16)
    nblk = fd // BLK
    code_rows = 8
    code = jnp.concatenate(
        [own_blocks // 8, own_blocks % 8, jnp.zeros((n_loc, BLK - 2 * FBLK), jnp.int32)], axis=1
    ).astype(jnp.bfloat16)
    code = jnp.concatenate(
        [code[:, None, :], jnp.zeros((n_loc, code_rows - 1, BLK), jnp.bfloat16)], axis=1
    )
    blocks_major = projected.reshape(n_loc, nosv, nblk, BLK).transpose(0, 2, 1, 3)
    payload = jnp.concatenate([blocks_major.reshape(n_loc, nblk * nosv, BLK), code], axis=1)
    which = jnp.sum(sel.astype(jnp.int32) * jnp.arange(n_loc)[None, None, :], axis=2)
    send = jnp.take(payload, which.reshape(-1), axis=0, mode="clip").reshape(ngroups, CAP, *payload.shape[1:])
    recv = lax.all_to_all(send, "orb", split_axis=0, concat_axis=0, tiled=True)
    recv = recv.reshape(ngroups * CAP, nblk * nosv + code_rows, BLK)
    my_owner = lax.dynamic_index_in_dim(owner, me, 0, keepdims=False)
    my_rank = lax.dynamic_index_in_dim(rank, me, 0, keepdims=False)
    slot = (my_owner * CAP + my_rank).astype(jnp.int32)
    pick = (slot[:, None] == jnp.arange(ngroups * CAP)[None, :]).astype(jnp.float32)
    codes = recv[:, nblk * nosv, : 2 * FBLK].astype(jnp.float32)
    pcode = jnp.einsum("ns,sc->nc", pick, codes)
    pblocks = (pcode[:, :FBLK] * 8 + pcode[:, FBLK:]).astype(jnp.int32)
    match = pblocks[:, None, None, :] == own_blocks[None, :, :, None]
    bidx = jnp.sum(jnp.where(match, jnp.arange(1, FBLK + 1)[None, None, :, None], 0), axis=2) - 1
    pair = pair_call(slot, bidx.astype(jnp.int32).reshape(-1), blocks_major, recv)
    return pair.reshape(1, n_loc, npart, nosv * nosv)


def make_pair_call(npb):
    def pair_kernel(slot_ref, bidx_ref, own_ref, recv_ref, out_ref, al_ref):
        g = pl.program_id(0)
        n_loc, nblk, nosv, _ = own_ref.shape
        for j in range(npb):
            n = g * npb + j
            s = slot_ref[n]
            for r in range(n_loc):
                for e in range(nblk):
                    b = bidx_ref[(n * n_loc + r) * nblk + e]
                    blk = own_ref[r, jnp.maximum(b, 0)]
                    blk = jnp.where(b >= 0, blk, jnp.zeros_like(blk))
                    al_ref[j, r * nosv : (r + 1) * nosv, e * BLK : (e + 1) * BLK] = blk
            part = jnp.concatenate(
                [recv_ref[s, e * nosv : (e + 1) * nosv, :] for e in range(nblk)], axis=1
            )
            res = lax.dot_general(
                al_ref[j], part, (((1,), (1,)), ((), ())), preferred_element_type=jnp.float32
            )
            out_ref[:, j] = res.reshape(n_loc, nosv, nosv).astype(out_ref.dtype)

    def pair_call(slot, bidx, own_bm, recv):
        n_loc, nblk, nosv, _ = own_bm.shape
        npart = slot.shape[0]
        nslot, rows, _ = recv.shape
        return pl.pallas_call(
            pair_kernel,
            out_shape=jax.ShapeDtypeStruct((n_loc, npart, nosv, nosv), jnp.bfloat16),
            grid_spec=pltpu.PrefetchScalarGridSpec(
                num_scalar_prefetch=2,
                grid=(npart // npb,),
                in_specs=[
                    pl.BlockSpec((n_loc, nblk, nosv, BLK), lambda g, s, b: (0, 0, 0, 0)),
                    pl.BlockSpec((nslot, rows, BLK), lambda g, s, b: (0, 0, 0)),
                ],
                out_specs=pl.BlockSpec((n_loc, npb, nosv, nosv), lambda g, s, b: (0, g, 0, 0)),
                scratch_shapes=[pltpu.VMEM((npb, n_loc * nosv, nblk * BLK), jnp.bfloat16)],
            ),
        )(slot, bidx, own_bm, recv)

    return pair_call


pair_call = make_pair_call(4)


def solution(mesh):
    nfit = mesh.shape["fit"]
    norb = mesh.shape["orb"]
    devs = np.asarray(mesh.devices).reshape(nfit // 2, 2, norb)
    mesh3 = Mesh(devs, ("z", "core", "orb"))
    fit = ("z", "core")
    return jax.shard_map(
        per_device,
        mesh=mesh3,
        in_specs=(
            P("orb", None, fit, None),
            P("orb", fit, None, None),
            P("orb", fit, None),
            P(fit, None, None),
        ),
        out_specs=P("orb", fit, None, None),
        check_vma=False,
    )
```

```python
import functools
import jax
import jax.numpy as jnp
import numpy as np
from jax import lax
from jax.experimental import pallas as pl
from jax.experimental.pallas import tpu as pltpu
from jax.sharding import Mesh, PartitionSpec as P

BLK = 128
FBLK = 6
CAP = 3
ORB_DEV = 8


def per_device(half_ints, osv_coef, fit_blocks, partner_list):
    nz = lax.axis_size("z")
    ncore = lax.axis_size("core")
    rows = half_ints[0]
    n_orb, fchunk, aod = rows.shape
    rows = rows.reshape(nz, ncore, n_orb // (nz * ncore), fchunk, aod)
    mine = lax.all_to_all(rows, "core", split_axis=1, concat_axis=3, tiled=True)
    mine = mine.reshape(nz, n_orb // (nz * ncore), ncore * fchunk, aod)
    coef = lax.all_gather(osv_coef[0], "z", axis=0, tiled=False)
    part = jnp.einsum(
        "zkfm,zkma->zkaf", mine, coef, preferred_element_type=jnp.float32
    ).astype(jnp.bfloat16)
    projected = lax.all_to_all(part, "z", split_axis=0, concat_axis=3, tiled=True)[0]
    n_loc, nosv, fd = projected.shape

    own_blocks = fit_blocks[0]
    lists = partner_list[0]
    ngroups, npart = lists.shape
    owner = lists // ORB_DEV
    sub = lists % ORB_DEV
    earlier = jnp.tril(jnp.ones((npart, npart), jnp.int32), -1)
    same = (owner[:, :, None] == owner[:, None, :]).astype(jnp.int32)
    rank = jnp.sum(same * earlier[None], axis=2)
    me = lax.axis_index("orb")
    sel = (
        (owner == me)[:, :, None, None]
        & (rank[:, :, None, None] == jnp.arange(CAP)[None, None, :, None])
        & (sub[:, :, None, None] == jnp.arange(n_loc)[None, None, None, :])
    )
    sel = jnp.sum(sel.astype(jnp.float32), axis=1).astype(jnp.bfloat16)
    nblk = fd // BLK
    code_rows = 8
    code = jnp.concatenate(
        [own_blocks // 8, own_blocks % 8, jnp.zeros((n_loc, BLK - 2 * FBLK), jnp.int32)], axis=1
    ).astype(jnp.bfloat16)
    code = jnp.concatenate(
        [code[:, None, :], jnp.zeros((n_loc, code_rows - 1, BLK), jnp.bfloat16)], axis=1
    )
    blocks_major = projected.reshape(n_loc, nosv, nblk, BLK).transpose(0, 2, 1, 3)
    payload = jnp.concatenate([blocks_major.reshape(n_loc, nblk * nosv, BLK), code], axis=1)
    which = jnp.sum(sel.astype(jnp.int32) * jnp.arange(n_loc)[None, None, :], axis=2)
    send = jnp.take(payload, which.reshape(-1), axis=0, mode="clip").reshape(ngroups, CAP, *payload.shape[1:])
    recv = lax.all_to_all(send, "orb", split_axis=0, concat_axis=0, tiled=True)
    recv = recv.reshape(ngroups * CAP, nblk * nosv + code_rows, BLK)
    my_owner = lax.dynamic_index_in_dim(owner, me, 0, keepdims=False)
    my_rank = lax.dynamic_index_in_dim(rank, me, 0, keepdims=False)
    slot = (my_owner * CAP + my_rank).astype(jnp.int32)
    pick = (slot[:, None] == jnp.arange(ngroups * CAP)[None, :]).astype(jnp.float32)
    codes = recv[:, nblk * nosv, : 2 * FBLK].astype(jnp.float32)
    pcode = jnp.einsum("ns,sc->nc", pick, codes)
    pblocks = (pcode[:, :FBLK] * 8 + pcode[:, FBLK:]).astype(jnp.int32)
    match = pblocks[:, None, None, :] == own_blocks[None, :, :, None]
    bidx = jnp.sum(jnp.where(match, jnp.arange(1, FBLK + 1)[None, None, :, None], 0), axis=2) - 1
    pair = pair_call(slot, bidx.astype(jnp.int32).reshape(-1), blocks_major, recv)
    return pair.reshape(1, n_loc, npart, nosv * nosv)


def make_pair_call(npb):
    def pair_kernel(slot_ref, bidx_ref, own_ref, recv_ref, out_ref, al_ref, res_ref):
        g = pl.program_id(0)
        n_loc, nblk, nosv, _ = own_ref.shape
        for j in range(npb):
            n = g * npb + j
            s = slot_ref[n]
            for r in range(n_loc):
                for e in range(nblk):
                    b = bidx_ref[(n * n_loc + r) * nblk + e]
                    blk = own_ref[r, jnp.maximum(b, 0)]
                    blk = jnp.where(b >= 0, blk, jnp.zeros_like(blk))
                    al_ref[j, r * nosv : (r + 1) * nosv, e * BLK : (e + 1) * BLK] = blk
            part = jnp.concatenate(
                [recv_ref[s, e * nosv : (e + 1) * nosv, :] for e in range(nblk)], axis=1
            )
            res = lax.dot_general(
                al_ref[j], part, (((1,), (1,)), ((), ())), preferred_element_type=jnp.float32
            )
            res_ref[j] = res
            even = res_ref[j, pl.ds(0, n_loc * nosv // 2, stride=2), :]
            odd = res_ref[j, pl.ds(1, n_loc * nosv // 2, stride=2), :]
            both = jnp.concatenate([even, odd], axis=1)
            out_ref[:, j] = both.reshape(n_loc, nosv // 2, 2 * nosv).astype(out_ref.dtype)

    def pair_call(slot, bidx, own_bm, recv):
        n_loc, nblk, nosv, _ = own_bm.shape
        npart = slot.shape[0]
        nslot, rows, _ = recv.shape
        return pl.pallas_call(
            pair_kernel,
            out_shape=jax.ShapeDtypeStruct((n_loc, npart, nosv // 2, 2 * nosv), jnp.bfloat16),
            grid_spec=pltpu.PrefetchScalarGridSpec(
                num_scalar_prefetch=2,
                grid=(npart // npb,),
                in_specs=[
                    pl.BlockSpec((n_loc, nblk, nosv, BLK), lambda g, s, b: (0, 0, 0, 0)),
                    pl.BlockSpec((nslot, rows, BLK), lambda g, s, b: (0, 0, 0)),
                ],
                out_specs=pl.BlockSpec((n_loc, npb, nosv // 2, 2 * nosv), lambda g, s, b: (0, g, 0, 0)),
                scratch_shapes=[
                    pltpu.VMEM((npb, n_loc * nosv, nblk * BLK), jnp.bfloat16),
                    pltpu.VMEM((npb, n_loc * nosv, nosv), jnp.float32),
                ],
            ),
        )(slot, bidx, own_bm, recv)

    return pair_call


pair_call = make_pair_call(4)


def solution(mesh):
    nfit = mesh.shape["fit"]
    norb = mesh.shape["orb"]
    devs = np.asarray(mesh.devices).reshape(nfit // 2, 2, norb)
    mesh3 = Mesh(devs, ("z", "core", "orb"))
    fit = ("z", "core")
    return jax.shard_map(
        per_device,
        mesh=mesh3,
        in_specs=(
            P("orb", None, fit, None),
            P("orb", fit, None, None),
            P("orb", fit, None),
            P(fit, None, None),
        ),
        out_specs=P("orb", fit, None, None),
        check_vma=False,
    )
```

```python
import functools
import jax
import jax.numpy as jnp
import numpy as np
from jax import lax
from jax.experimental import pallas as pl
from jax.experimental.pallas import tpu as pltpu
from jax.sharding import Mesh, PartitionSpec as P

BLK = 128
FBLK = 6
CAP = 3
ORB_DEV = 8


def per_device(half_ints, osv_coef, fit_blocks, partner_list):
    nz = lax.axis_size("z")
    ncore = lax.axis_size("core")
    rows = half_ints[0]
    n_orb, fchunk, aod = rows.shape
    rows = rows.reshape(nz, ncore, n_orb // (nz * ncore), fchunk, aod)
    mine = lax.all_to_all(rows, "core", split_axis=1, concat_axis=3, tiled=True)
    mine = mine.reshape(nz, n_orb // (nz * ncore), ncore * fchunk, aod)
    coef = lax.all_gather(osv_coef[0], "z", axis=0, tiled=False)
    part = jnp.einsum(
        "zkfm,zkma->zkaf", mine, coef, preferred_element_type=jnp.float32
    ).astype(jnp.bfloat16)
    projected = lax.all_to_all(part, "z", split_axis=0, concat_axis=3, tiled=True)[0]
    n_loc, nosv, fd = projected.shape

    own_blocks = fit_blocks[0]
    lists = partner_list[0]
    ngroups, npart = lists.shape
    owner = lists // ORB_DEV
    sub = lists % ORB_DEV
    earlier = jnp.tril(jnp.ones((npart, npart), jnp.int32), -1)
    same = (owner[:, :, None] == owner[:, None, :]).astype(jnp.int32)
    rank = jnp.sum(same * earlier[None], axis=2)
    me = lax.axis_index("orb")
    sel = (
        (owner == me)[:, :, None, None]
        & (rank[:, :, None, None] == jnp.arange(CAP)[None, None, :, None])
        & (sub[:, :, None, None] == jnp.arange(n_loc)[None, None, None, :])
    )
    sel = jnp.sum(sel.astype(jnp.float32), axis=1).astype(jnp.bfloat16)
    nblk = fd // BLK
    code_rows = 8
    code = jnp.concatenate(
        [own_blocks // 8, own_blocks % 8, jnp.zeros((n_loc, BLK - 2 * FBLK), jnp.int32)], axis=1
    ).astype(jnp.bfloat16)
    code = jnp.concatenate(
        [code[:, None, :], jnp.zeros((n_loc, code_rows - 1, BLK), jnp.bfloat16)], axis=1
    )
    blocks_major = projected.reshape(n_loc, nosv, nblk, BLK).transpose(0, 2, 1, 3)
    payload = jnp.concatenate([blocks_major.reshape(n_loc, nblk * nosv, BLK), code], axis=1)
    which = jnp.sum(sel.astype(jnp.int32) * jnp.arange(n_loc)[None, None, :], axis=2)
    send = jnp.take(payload, which.reshape(-1), axis=0, mode="clip").reshape(ngroups, CAP, *payload.shape[1:])
    recv = lax.all_to_all(send, "orb", split_axis=0, concat_axis=0, tiled=True)
    recv = recv.reshape(ngroups * CAP, nblk * nosv + code_rows, BLK)
    my_owner = lax.dynamic_index_in_dim(owner, me, 0, keepdims=False)
    my_rank = lax.dynamic_index_in_dim(rank, me, 0, keepdims=False)
    slot = (my_owner * CAP + my_rank).astype(jnp.int32)
    pick = (slot[:, None] == jnp.arange(ngroups * CAP)[None, :]).astype(jnp.float32)
    codes = recv[:, nblk * nosv, : 2 * FBLK].astype(jnp.float32)
    pcode = jnp.einsum("ns,sc->nc", pick, codes)
    pblocks = (pcode[:, :FBLK] * 8 + pcode[:, FBLK:]).astype(jnp.int32)
    match = pblocks[:, None, None, :] == own_blocks[None, :, :, None]
    bidx = jnp.sum(jnp.where(match, jnp.arange(1, FBLK + 1)[None, None, :, None], 0), axis=2) - 1
    bidx = jnp.where(bidx < 0, FBLK, bidx)
    own_pad = jnp.concatenate([blocks_major, jnp.zeros_like(blocks_major[:, :1])], axis=1)
    pair = pair_call(slot, bidx.astype(jnp.int32).reshape(-1), own_pad, recv)
    return pair.reshape(1, n_loc, npart, nosv * nosv)


def make_pair_call(npb):
    def pair_kernel(slot_ref, bidx_ref, own_ref, recv_ref, out_ref, al_ref, res_ref):
        g = pl.program_id(0)
        n_loc, nblk, nosv, _ = own_ref.shape
        nblk -= 1
        for j in range(npb):
            n = g * npb + j
            s = slot_ref[n]
            for r in range(n_loc):
                for e in range(nblk):
                    b = bidx_ref[(n * n_loc + r) * nblk + e]
                    blk = own_ref[r, b]
                    al_ref[j, r * nosv : (r + 1) * nosv, e * BLK : (e + 1) * BLK] = blk
            part = jnp.concatenate(
                [recv_ref[s, e * nosv : (e + 1) * nosv, :] for e in range(nblk)], axis=1
            )
            res = lax.dot_general(
                al_ref[j], part, (((1,), (1,)), ((), ())), preferred_element_type=jnp.float32
            )
            res_ref[j] = res
            even = res_ref[j, pl.ds(0, n_loc * nosv // 2, stride=2), :]
            odd = res_ref[j, pl.ds(1, n_loc * nosv // 2, stride=2), :]
            both = jnp.concatenate([even, odd], axis=1)
            out_ref[:, j] = both.reshape(n_loc, nosv // 2, 2 * nosv).astype(out_ref.dtype)

    def pair_call(slot, bidx, own_bm, recv):
        n_loc, nblk, nosv, _ = own_bm.shape
        npart = slot.shape[0]
        nslot, rows, _ = recv.shape
        return pl.pallas_call(
            pair_kernel,
            out_shape=jax.ShapeDtypeStruct((n_loc, npart, nosv // 2, 2 * nosv), jnp.bfloat16),
            grid_spec=pltpu.PrefetchScalarGridSpec(
                num_scalar_prefetch=2,
                grid=(npart // npb,),
                in_specs=[
                    pl.BlockSpec(own_bm.shape, lambda g, s, b: (0, 0, 0, 0)),
                    pl.BlockSpec((nslot, rows, BLK), lambda g, s, b: (0, 0, 0)),
                ],
                out_specs=pl.BlockSpec((n_loc, npb, nosv // 2, 2 * nosv), lambda g, s, b: (0, g, 0, 0)),
                scratch_shapes=[
                    pltpu.VMEM((npb, n_loc * nosv, (nblk - 1) * BLK), jnp.bfloat16),
                    pltpu.VMEM((npb, n_loc * nosv, nosv), jnp.float32),
                ],
            ),
        )(slot, bidx, own_bm, recv)

    return pair_call


pair_call = make_pair_call(8)


def solution(mesh):
    nfit = mesh.shape["fit"]
    norb = mesh.shape["orb"]
    devs = np.asarray(mesh.devices).reshape(nfit // 2, 2, norb)
    mesh3 = Mesh(devs, ("z", "core", "orb"))
    fit = ("z", "core")
    return jax.shard_map(
        per_device,
        mesh=mesh3,
        in_specs=(
            P("orb", None, fit, None),
            P("orb", fit, None, None),
            P("orb", fit, None),
            P(fit, None, None),
        ),
        out_specs=P("orb", fit, None, None),
        check_vma=False,
    )
```
